32 devices in a mesh: groups: 2 (over x), ctx: 8 (over z, y), head: 2 (over core).
Axes of the slice: x: 2, y: 2, z: 4, core: 2. Of those that a mesh axis runs over, the one named last changes fastest.
Arguments:
- queries: bfloat16 [8192, 1024], P(('groups', 'ctx'), 'head'), parts along dimension 0, may hold values from -6 to 6
- keys: bfloat16 [8192, 1024], P(('groups', 'ctx'), 'head'), parts along dimension 0, may hold values from -6 to 6
- values: bfloat16 [8192, 2048], P(('groups', 'ctx'), 'head'), parts along dimension 0, may hold values from -30 to 30
- in_gate: float32 [4, 8192], P('head', ('groups', 'ctx')), parts along dimension 1, may hold values from -60 to 150
- forget_gate: float32 [4, 8192], P('head', ('groups', 'ctx')), parts along dimension 1, may hold values from -5 to 16
- w_out: bfloat16 [2048, 4096], P('head'), may hold values from -0.125 to 0.125
Outputs:
- layer_out: bfloat16 [8192, 4096], P(('groups', 'ctx', 'head')), parts along dimension 0
The draws below stay inside these ranges and needn't reach their ends.
There are 2 independent parts, one for each index of `groups`. The reference program is written for one: setup_inputs(seed, part) draws one part's arguments, and reference() takes and returns one part's arrays. A program takes and returns all parts, laid end to end along the dimension named above; an argument that names none is the same for every part. Nothing has to cross between parts.
All inputs are finite; a program needn't handle non-finite values.
Results may differ from the reference program's by a relative error of at most 0.009.
Values may be sent and summed in bfloat16 or wider, within the bound.
No kernel may reach another device: no remote copies, remote signals or barrier semaphores. Data moves between devices by JAX's collectives and lax.ppermute only.
A program may use at most 192 MiB of HBM per device.

```python
import jax
import jax.numpy as jnp
from jax import lax

D = 4096
LOCAL_HEADS = 4
DK = 256
DV = 512
TOK_DEV = 512
SLAB_LENGTH = 4096
N_CTX = 8


def spread_blocks(block_values):
    return jnp.repeat(block_values, TOK_DEV, axis=1)


def draw_forget_gate(key, part):
    random_subkeys = jax.random.split(jax.random.fold_in(key, 101), 5)
    block_count = SLAB_LENGTH // TOK_DEV
    ranking = jax.random.permutation(random_subkeys[0], LOCAL_HEADS)
    keeping = ranking < LOCAL_HEADS // 2
    factor = spread_blocks(jax.random.uniform(random_subkeys[1], (LOCAL_HEADS, block_count), jnp.float32, 1.0, 2.5))
    jitter = jax.random.uniform(random_subkeys[2], (LOCAL_HEADS, SLAB_LENGTH), jnp.float32, 0.5, 1.5)
    fast_rate = 8.0 / TOK_DEV
    slow_rate = 0.25 / SLAB_LENGTH
    decay_speed = jnp.where(keeping[:, None], slow_rate, fast_rate) * factor * jitter
    spike_locations = jax.random.randint(random_subkeys[3], (LOCAL_HEADS, 2), 0, SLAB_LENGTH)
    decay_losses = jax.random.uniform(random_subkeys[4], (LOCAL_HEADS, 2), jnp.float32, 0.2, 0.5)
    spike_positions = jnp.arange(SLAB_LENGTH)[None, None, :] == spike_locations[:, :, None]
    spike_values = jnp.sum(jnp.where(spike_positions, jnp.log1p(-decay_losses)[:, :, None], 0.0), axis=1)
    forget_logarithm = spike_values - decay_speed
    return forget_logarithm - jnp.log(-jnp.expm1(forget_logarithm))


def draw_in_gate(key, part):
    random_subkeys = jax.random.split(jax.random.fold_in(key, 202), 2)
    block_count = SLAB_LENGTH // TOK_DEV
    offsets = spread_blocks(jax.random.uniform(random_subkeys[0], (LOCAL_HEADS, block_count), jnp.float32, -2.0, 2.0))
    gate_values = jnp.clip(2.0 * jax.random.normal(random_subkeys[1], (LOCAL_HEADS, SLAB_LENGTH), jnp.float32) + offsets, -12.0, 12.0)
    return gate_values


def draw_values(key, part):
    random_subkeys = jax.random.split(jax.random.fold_in(key, 303), 3)
    feature_count = LOCAL_HEADS * DV
    row_scale = jnp.exp(jax.random.uniform(random_subkeys[0], (SLAB_LENGTH, 1), jnp.float32, -1.15, 1.15))
    column_scale = jnp.exp(jax.random.uniform(random_subkeys[1], (1, feature_count), jnp.float32, -1.15, 1.15))
    entries = jax.random.normal(random_subkeys[2], (SLAB_LENGTH, feature_count), jnp.float32)
    return jnp.clip(entries * row_scale * column_scale, -30.0, 30.0).astype(jnp.bfloat16)


def steps_of(stream_key, extent, shards, least, high):
    gain = 1.0
    for axis_at, blocks in shards:
        steps = jax.random.uniform(jax.random.fold_in(jax.random.fold_in(stream_key, 6), axis_at), (blocks,), jnp.float32, least / len(shards), high / len(shards))
        gain = gain * jnp.repeat(jnp.exp(steps), extent[axis_at] // blocks).reshape((-1,) + (1,) * (len(extent) - 1 - axis_at))
    return gain


def centred(own_key, shape, deviation, reach, cuts=(), kind=jnp.bfloat16):
    factor_of = steps_of(own_key, shape, cuts, -0.22, 0.18) if cuts else 1.0
    values = jax.random.normal(own_key, shape, jnp.float32) * deviation * factor_of
    return jnp.minimum(jnp.maximum(values, -reach), reach).astype(kind)


def setup_inputs(seed: int = 0, part: int = 0) -> dict:
    arg_keys = jax.random.split(jax.random.key(seed), 7)
    own_keys = jax.random.split(jax.random.fold_in(arg_keys[6], part), 7)
    queries = centred(own_keys[0], (SLAB_LENGTH, LOCAL_HEADS * DK), 1.0, 6.0, ((0, 8), (1, 2)))
    keys = centred(own_keys[1], (SLAB_LENGTH, LOCAL_HEADS * DK), 1.0, 6.0, ((0, 8), (1, 2)))
    values = draw_values(jax.random.fold_in(jax.random.fold_in(arg_keys[6], part), 71), part)
    in_gate = draw_in_gate(jax.random.fold_in(jax.random.fold_in(arg_keys[6], part), 71), part)
    forget_gate = draw_forget_gate(jax.random.fold_in(jax.random.fold_in(arg_keys[6], part), 71), part)
    w_out = centred(arg_keys[5], (LOCAL_HEADS * DV, D), (LOCAL_HEADS * DV) ** -0.5, 0.125, ((0, 2),))
    return {"queries": queries, "keys": keys, "values": values, "in_gate": in_gate, "forget_gate": forget_gate, "w_out": w_out}


norm_epsilon = 1e-06
very_negative = -1e+30

def reference(queries, keys, values, in_gate, forget_gate, w_out):
    block_count = N_CTX
    score_scale = DK ** (-0.5)
    query_blocks = queries.reshape(block_count, TOK_DEV, LOCAL_HEADS, DK)
    key_blocks = keys.reshape(block_count, TOK_DEV, LOCAL_HEADS, DK)
    value_blocks = values.reshape(block_count, TOK_DEV, LOCAL_HEADS, DV)
    input_blocks = in_gate.reshape(LOCAL_HEADS, block_count, TOK_DEV).transpose(1, 0, 2)
    forget_blocks = forget_gate.reshape(LOCAL_HEADS, block_count, TOK_DEV).transpose(1, 0, 2)
    causal = jnp.arange(TOK_DEV)[:, None] >= jnp.arange(TOK_DEV)[None, :]

    def advance(carried, segment):
        prev_max, previous_state = carried
        query_per_head, key_heads, value_per_head, input_log, forget_pre = segment
        running = jnp.cumsum(jax.nn.log_sigmoid(forget_pre), axis=1)
        decay_total = running[:, -1]
        tail_log = decay_total[:, None] - running + input_log
        local_max = lax.optimization_barrier(jnp.max(tail_log, axis=1))
        key_scaled_rows = (key_heads.astype(jnp.float32) * jnp.exp(tail_log - local_max[:, None]).T[:, :, None]).astype(jnp.bfloat16)
        segment_state = jnp.einsum('ben,bet->ent', key_scaled_rows.astype(jnp.float32), value_per_head.astype(jnp.float32))
        scores = jnp.einsum('thk,shk->hts', query_per_head.astype(jnp.float32), key_heads.astype(jnp.float32)) * score_scale
        log_weight = jnp.where(causal[None], running[:, :, None] - running[:, None, :] + input_log[:, None, :], -jnp.inf)
        carry_log = running + prev_max[:, None]
        stabilizer = jnp.maximum(lax.optimization_barrier(jnp.max(log_weight, axis=2)), carry_log)
        weights = (jnp.exp(log_weight - stabilizer[:, :, None]) * scores).astype(jnp.bfloat16)
        local_term = jnp.einsum('hts,shv->thv', weights.astype(jnp.float32), value_per_head.astype(jnp.float32))
        carryover_term = jnp.einsum('raq,aqy->ray', query_per_head.astype(jnp.float32), previous_state, precision=lax.Precision.HIGHEST)
        hidden = local_term + carryover_term * (score_scale * jnp.exp(carry_log - stabilizer)).T[:, :, None]
        normed = hidden * lax.rsqrt(lax.optimization_barrier(jnp.mean(hidden * hidden, axis=2, keepdims=True)) + norm_epsilon)
        mixed = normed.astype(jnp.bfloat16).reshape(TOK_DEV, LOCAL_HEADS * DV)
        block_out = jnp.dot(mixed, w_out, preferred_element_type=jnp.float32).astype(jnp.bfloat16)
        joined = jnp.maximum(prev_max + decay_total, local_max)
        next_state = jnp.exp(prev_max + decay_total - joined)[:, None, None] * previous_state + jnp.exp(local_max - joined)[:, None, None] * segment_state
        return ((joined, next_state), block_out)
    initial = (jnp.full((LOCAL_HEADS,), very_negative, jnp.float32), jnp.zeros((LOCAL_HEADS, DK, DV), jnp.float32))
    final_carry, outputs = lax.scan(advance, initial, (query_blocks, key_blocks, value_blocks, input_blocks, forget_blocks))
    return outputs.reshape(block_count * TOK_DEV, D)
```

```python
import jax
import jax.numpy as jnp
from jax import lax
from jax.sharding import PartitionSpec as P

DK = 256
DV = 512


norm_epsilon = 1e-06
very_negative = -1e30


def join_states(earlier, latter):
    decay_first, max_first, state_first = earlier
    decay_second, max_second, state_second = latter
    joined = jnp.maximum(max_first + decay_second, max_second)
    merged = (
        jnp.exp(max_first + decay_second - joined)[:, None, None] * state_first
        + jnp.exp(max_second - joined)[:, None, None] * state_second
    )
    return (decay_first + decay_second, joined, merged)


def exclusive_prefix(own, ctx_count):
    place = lax.axis_index("ctx")
    decay, top, state = own
    head_count = decay.shape[0]
    covered = (decay, top, state)
    earlier = (
        jnp.zeros((head_count,), jnp.float32),
        jnp.full((head_count,), very_negative, jnp.float32),
        jnp.zeros_like(state),
    )
    shift = 1
    while shift < ctx_count:
        pairs = [(i, i + shift) for i in range(ctx_count - shift)]
        scalars = lax.ppermute(jnp.stack([covered[0], covered[1]]), "ctx", pairs)
        got_state = lax.ppermute(covered[2], "ctx", pairs)
        valid = place >= shift
        got = (
            jnp.where(valid, scalars[0], 0.0),
            jnp.where(valid, scalars[1], very_negative),
            got_state,
        )
        earlier = join_states(got, earlier)
        if 2 * shift < ctx_count:
            covered = join_states(got, covered)
        shift *= 2
    return earlier


def make_body(ctx_count, head_axis_count):
    def body(queries, keys, values, in_gate, forget_gate, w_out):
        row_count = queries.shape[0]
        head_count = in_gate.shape[0]
        score_scale = DK ** (-0.5)
        query_per_head = queries.reshape(row_count, head_count, DK)
        key_heads = keys.reshape(row_count, head_count, DK)
        value_per_head = values.reshape(row_count, head_count, DV)
        running = jnp.cumsum(jax.nn.log_sigmoid(forget_gate), axis=1)
        decay_total = running[:, -1]
        tail_log = decay_total[:, None] - running + in_gate
        local_max = jnp.max(tail_log, axis=1)
        key_scaled_rows = (
            key_heads * jnp.exp(tail_log - local_max[:, None]).T[:, :, None]
        ).astype(jnp.bfloat16)
        segment_state = jnp.einsum(
            "ben,bet->ent", key_scaled_rows, value_per_head, preferred_element_type=jnp.float32
        )
        scanned = exclusive_prefix((decay_total, local_max, segment_state), ctx_count)
        prev_max = scanned[1]
        previous_state = scanned[2]
        causal = jnp.arange(row_count)[:, None] >= jnp.arange(row_count)[None, :]
        scores = (
            jnp.einsum("thk,shk->hts", query_per_head, key_heads, preferred_element_type=jnp.float32)
            * score_scale
        )
        log_weight = jnp.where(
            causal[None], running[:, :, None] - running[:, None, :] + in_gate[:, None, :], -jnp.inf
        )
        carry_log = running + prev_max[:, None]
        stabilizer = jnp.maximum(jnp.max(log_weight, axis=2), carry_log)
        weights = (jnp.exp(log_weight - stabilizer[:, :, None]) * scores).astype(jnp.bfloat16)
        local_term = jnp.einsum(
            "hts,shv->thv", weights, value_per_head, preferred_element_type=jnp.float32
        )
        carryover_term = jnp.einsum(
            "raq,aqy->ray",
            query_per_head.astype(jnp.float32),
            previous_state,
            precision=lax.Precision.HIGHEST,
        )
        hidden = (
            local_term
            + carryover_term * (score_scale * jnp.exp(carry_log - stabilizer)).T[:, :, None]
        )
        normed = hidden * lax.rsqrt(jnp.mean(hidden * hidden, axis=2, keepdims=True) + norm_epsilon)
        mixed = normed.astype(jnp.bfloat16).reshape(row_count, head_count * DV)
        if head_axis_count != 2:
            return lax.psum_scatter(
                jnp.dot(mixed, w_out, preferred_element_type=jnp.float32).astype(jnp.bfloat16),
                "head",
                scatter_dimension=0,
                tiled=True,
            )
        core = lax.axis_index("head")
        half = row_count // 2
        peer_rows = lax.dynamic_slice_in_dim(mixed, (1 - core) * half, half, 0)
        own_rows = lax.dynamic_slice_in_dim(mixed, core * half, half, 0)
        peer_part = jnp.dot(peer_rows, w_out, preferred_element_type=jnp.float32).astype(
            jnp.bfloat16
        )
        received = lax.ppermute(peer_part, "head", [(0, 1), (1, 0)])
        own_part = jnp.dot(own_rows, w_out, preferred_element_type=jnp.float32)
        return (own_part + received.astype(jnp.float32)).astype(jnp.bfloat16)

    return body


def solution(mesh):
    return jax.shard_map(
        make_body(mesh.shape["ctx"], mesh.shape["head"]),
        mesh=mesh,
        in_specs=(
            P(("groups", "ctx"), "head"),
            P(("groups", "ctx"), "head"),
            P(("groups", "ctx"), "head"),
            P("head", ("groups", "ctx")),
            P("head", ("groups", "ctx")),
            P("head", None),
        ),
        out_specs=P(("groups", "ctx", "head"), None),
        check_vma=False,
    )
```
